512 devices in a mesh: table: 64 (over y, z), expert: 8 (over x, core).
Axes of the slice: x: 4, y: 8, z: 8, core: 2. Of those that a mesh axis runs over, the one named last changes fastest.
Arguments:
- table: bfloat16 [64, 512, 256], P('table'), may hold values from -127 to 127, as said below
- row_scale: float32 [64, 512], P('table'), may hold values from 0.3 to 3
- windows: int32 [64, 8, 256], P('table', 'expert'), may hold values from 0 to 511, as said below
- bag_idx: int32 [64, 8, 8192, 8], P('table', 'expert'), may hold values from 0 to 255
- bag_len: int32 [64, 8, 8192], P('table', 'expert'), may hold values from 1 to 8
- feat_gain: float32 [64, 256], replicated, may hold values from 0.03 to 0.3
- norm_gain: float32 [256], replicated, may hold values from 0.5 to 1.5
- expert_ids: int32 [8, 8192, 1], P('expert', 'table'), may hold values from 0 to 63; in each aligned block of 128 rows (0 to 127, 128 to 255, ..., all dimensions but the last counted through in order) at most 4 rows name the same one
- w_in: bfloat16 [64, 256, 4096], P('table', None, 'expert'), may hold values from -0.375 to 0.375
- w_out: bfloat16 [64, 4096, 256], P('table', 'expert'), may hold values from -0.09375 to 0.09375
- w_tow1: bfloat16 [3, 256, 256], replicated, may hold values from -0.375 to 0.375
- w_tow2: float32 [3, 256], replicated, may hold values from -1.5 to 1.5
- targets: float32 [8, 8192, 3], P('expert', 'table'), may hold values from 0 to 1
Outputs:
- predictions: float32 [8, 8192, 3], P('expert', 'table')
- grad_table: float32 [64, 512, 256], P('table', 'expert')
- grad_w_in: float32 [64, 256, 4096], P('table', None, 'expert')
- grad_w_out: float32 [64, 4096, 256], P('table', 'expert')
The draws below stay inside these ranges and needn't reach their ends.
Inputs may be any that keep to these rules, and one draw needn't show every extreme that they name: `table`: every entry is an integer. Each row windows[f, g] holds 256 distinct row numbers of feature f's table. `expert_ids`: in each aligned block of 128 samples (the samples of one device) no expert is named by more than 4 samples.
All inputs are finite; a program needn't handle non-finite values.
Results may differ from the reference program's by a relative error of at most 0.02.
Values may be sent and summed in bfloat16 or wider, within the bound.
No kernel may reach another device: no remote copies, remote signals or barrier semaphores. Data moves between devices by JAX's collectives and lax.ppermute only.
A program may use at most 128 MiB of HBM per device.

```python
import math
import jax
import jax.numpy as jnp
import numpy as np
from jax import lax

E = 256
FF = 4096
TH = 256
L = 8
WIN = 256
B_DEV = 128
TROWS = 512
F = 64
EXPERTS = 64
GROUPS = 8
B_GROUP = 8192
CAP = 4
N_EXPERT = 8


def draw_table(key, part):
    codes = jax.random.randint(jax.random.fold_in(key, 29), (F, TROWS, E), -127, 128)
    return codes.astype(jnp.float32).astype(jnp.bfloat16)


def draw_windows(key, part):
    keys = jax.random.split(jax.random.fold_in(key, 17), F * GROUPS)

    def one_window(subkey):
        return jax.random.permutation(subkey, TROWS)[:WIN]
    return jax.vmap(one_window)(keys).reshape(F, GROUPS, WIN).astype(jnp.int32)


def touch_ends(values, stream_key, least, largest):
    dims = values.shape
    spot = [jax.random.randint(jax.random.fold_in(stream_key, axis), (), 0, dims[axis]) for axis in range(len(dims))]
    values = values.at[tuple(spot)].set(least)
    longest = dims.index(max(dims))
    spot[longest] = (spot[longest] + 1) % dims[longest]
    return values.at[tuple(spot)].set(largest)


def block_levels(key, dims, cuts, low, largest):
    gain, own = 1.0, jax.random.fold_in(key, 6)
    for dim, blocks in cuts:
        heights = jnp.exp(jax.random.uniform(jax.random.fold_in(own, dim), (blocks,), jnp.float32, low / len(cuts), largest / len(cuts)))
        gain = gain * jnp.repeat(heights, dims[dim] // blocks).reshape([-1 if axis == dim else 1 for axis in range(len(dims))])
    return gain


def cumulative_ranks(count, lean):
    weights = [(1 << 20) // math.isqrt(grade ** lean) + 1 for grade in range(1, count + 1)]
    scale = 1 + sum(weights) // (1 << 30)
    return np.cumsum(np.array([max(1, weight // scale) for weight in weights]))


def ranked(own_key, dims, amount, slope):
    table = cumulative_ranks(amount, slope)
    ticket = jax.random.randint(jax.random.fold_in(own_key, 1), dims, 0, int(table[amount - 1]))
    grade = jnp.searchsorted(jnp.asarray(table, jnp.int32), ticket, side="right")
    return jax.random.permutation(jax.random.fold_in(own_key, 2), amount)[grade].astype(jnp.int32)


def shared_out(key, own, number, rows, amount, top, limit, slope):
    sequence = jax.random.permutation(key, amount)
    heavy_load, usual = shares(amount, rows * top, limit, slope, True), shares(amount, rows * top, limit, slope, False)
    places = jnp.arange(amount)

    def named(sizes, offset_by):
        used = int((sizes > 0).sum())
        fixed = max(1, used // 4)
        shifted = fixed + (places - fixed + offset_by * (used - fixed)) % max(1, amount - fixed)
        return jnp.zeros((amount,), jnp.int32).at[sequence[jnp.where(places < fixed, places, shifted)]].set(jnp.asarray(sizes, jnp.int32))

    sizes = jnp.where(number % 4 == 0, named(heavy_load, number // 4), named(usual, number - number // 4 - 1))
    mixed = jax.random.permutation(jax.random.fold_in(own, 3), amount)
    donor, taker = mixed[0:amount // 2 * 2:2], mixed[1:amount // 2 * 2:2]
    slack = jnp.minimum(sizes[donor] - 1, limit - sizes[taker]) // 2
    slack = jnp.where((donor == sequence[0]) | (taker == sequence[0]) | (sizes[taker] == 0), 0, jnp.maximum(slack, 0))
    shifted = jax.random.randint(jax.random.fold_in(own, 4), (amount // 2,), 0, 1 << 20) % (slack + 1)
    sizes = sizes.at[donor].add(-shifted).at[taker].add(shifted)
    labels = jnp.searchsorted(jnp.cumsum(sizes), jnp.arange(rows * top), side="right").astype(jnp.int32)
    grid = labels.reshape(top, rows).T
    grid = grid[jax.random.permutation(jax.random.fold_in(own, 1), rows)]
    offset_by = jax.random.randint(jax.random.fold_in(own, 2), (rows, 1), 0, top)
    return jnp.take_along_axis(grid, (jnp.arange(top)[None, :] + offset_by) % top, axis=1)


def shares(amount, total, reach, skew, full):
    portions = [(1 << 20) // math.isqrt(standing ** skew) + 1 for standing in range(1, amount + 1)]
    largest = reach if full else min(reach, max(-(-total // amount), total * portions[0] // sum(portions)))
    least = 1 if total - largest >= amount - 1 else 0
    counts, surplus = [largest] + [least] * (amount - 1), total - largest - least * (amount - 1)
    while surplus > 0:
        candidates = [i for i in range(1, amount) if counts[i] < largest] or [i for i in range(1, amount) if counts[i] < reach]
        pool, left = sum([portions[i] for i in candidates]), surplus
        for i in candidates:
            more = min(reach - counts[i], max(1, left * portions[i] // pool), surplus)
            counts[i] = counts[i] + more
            surplus = surplus - more
    return np.array(counts)


def scatter_about(stream_key, extent, scale, limit, cuts=(), kind=jnp.bfloat16):
    values = jax.random.normal(stream_key, extent, jnp.float32) * scale
    if len(cuts) > 0:
        values = block_levels(stream_key, extent, cuts, -0.22, 0.18) * values
    return jnp.clip(values, min=-limit, max=limit).astype(kind)


def setup_inputs(seed: int = 0) -> dict:
    streams_of = jax.random.split(jax.random.key(seed), 14)
    table = draw_table(jax.random.fold_in(streams_of[13], 71), 0)
    row_scale = jnp.clip(jnp.exp(math.log(3.0) - 2.3025851 * jax.random.uniform(streams_of[1], (F, TROWS), jnp.float32) ** block_levels(streams_of[1], (F, TROWS), ((0, 64),), -0.2, 0.2)), 0.3, 3.0)
    windows = draw_windows(jax.random.fold_in(streams_of[13], 71), 0)
    bag_idx = touch_ends(ranked(streams_of[3], (F, GROUPS, B_GROUP, L), WIN, 1), jax.random.fold_in(streams_of[3], 3), 0, WIN - 1).astype(jnp.int32)
    bag_len = touch_ends(jax.random.randint(streams_of[4], (F, GROUPS, B_GROUP), 1, L + 1), jax.random.fold_in(streams_of[4], 1), 1, L).astype(jnp.int32)
    feat_gain = jnp.clip(jnp.exp(jax.random.uniform(streams_of[5], (F, E), jnp.float32, math.log(0.03), math.log(0.3))), 0.03, 0.3)
    norm_gain = jnp.clip(1.0 + 0.1 * jax.random.normal(streams_of[6], (E,), jnp.float32), 0.5, 1.5)
    expert_ids_keys = jax.random.split(jax.random.fold_in(streams_of[7], 1), GROUPS * B_GROUP // B_DEV)
    expert_ids_turns = jax.random.permutation(jax.random.fold_in(streams_of[7], 3), GROUPS * B_GROUP // B_DEV)
    expert_ids = jax.vmap(lambda own, number: shared_out(jax.random.fold_in(streams_of[7], 2), own, number, B_DEV, EXPERTS, 1, CAP, 2))(expert_ids_keys, expert_ids_turns).reshape((GROUPS, B_GROUP, 1))
    w_in = scatter_about(streams_of[8], (EXPERTS, E, FF), E ** -0.5, 0.375, ((0, 64), (2, 8)))
    w_out = scatter_about(streams_of[9], (EXPERTS, FF, E), FF ** -0.5, 0.09375, ((0, 64), (1, 8)))
    w_tow1 = scatter_about(streams_of[10], (3, E, TH), E ** -0.5, 0.375)
    w_tow2 = scatter_about(streams_of[11], (3, TH), 0.25, 1.5, (), jnp.float32)
    targets = jnp.clip(1.0 * jax.random.uniform(streams_of[12], (GROUPS, B_GROUP, 3), jnp.float32) ** block_levels(streams_of[12], (GROUPS, B_GROUP, 3), ((0, 8), (1, 64)), -0.2, 0.2), 0.0, 1.0)
    return dict(table=table, row_scale=row_scale, windows=windows, bag_idx=bag_idx, bag_len=bag_len, feat_gain=feat_gain, norm_gain=norm_gain, expert_ids=expert_ids, w_in=w_in, w_out=w_out, w_tow1=w_tow1, w_tow2=w_tow2, targets=targets)


code_range = 127.0

def silu_slope(values):
    sigma = jax.nn.sigmoid(values)
    return sigma * (1.0 + values * (1.0 - sigma))

def rounded(values):
    return lax.optimization_barrier(values.astype(jnp.bfloat16)).astype(jnp.float32)

def column_partials(left, right):
    shard = FF // N_EXPERT
    left_split = left.astype(jnp.float32).reshape(left.shape[0], N_EXPERT, shard)
    right_split = right.astype(jnp.float32).reshape(N_EXPERT, shard, right.shape[-1])
    partials = jnp.einsum('rkf,kfe->kre', left_split, right_split)
    return lax.optimization_barrier(jnp.sum(rounded(partials), axis=0))

def reference(table, row_scale, windows, bag_idx, bag_len, feat_gain, norm_gain, expert_ids, w_in, w_out, w_tow1, w_tow2, targets):
    feature_ids = jnp.arange(F, dtype=jnp.int32)
    group_ids = jnp.arange(GROUPS, dtype=jnp.int32)
    picked = table[feature_ids[:, None, None], windows].astype(jnp.float32)
    scales = row_scale[feature_ids[:, None, None], windows]
    dequant = (picked * scales[..., None] / code_range).astype(jnp.bfloat16)
    slots = jnp.arange(L, dtype=jnp.int32)

    def live_mask(lengths):
        return (slots[None, :] < lengths[:, None]).astype(jnp.float32)

    def group_sum(group):

        def feature_step(carry, feature):
            rows = jnp.take(dequant[feature, group], bag_idx[feature, group], axis=0).astype(jnp.float32)
            pooled = lax.optimization_barrier(jnp.sum(rows * live_mask(bag_len[feature, group])[:, :, None], axis=1)).astype(jnp.bfloat16)
            return (carry + pooled.astype(jnp.float32) * feat_gain[feature], None)
        result, _ = lax.scan(feature_step, jnp.zeros((B_GROUP, E), jnp.float32), feature_ids)
        return result
    summed = lax.map(group_sum, group_ids).reshape(GROUPS * B_GROUP, E)
    inverse = lax.rsqrt(lax.optimization_barrier(jnp.mean(summed * summed, axis=-1, keepdims=True)) + 1e-05)
    normed = (summed * inverse * norm_gain).astype(jnp.bfloat16)
    blocks = GROUPS * B_GROUP // B_DEV
    chosen = expert_ids.reshape(blocks, B_DEV)
    member = (chosen[:, :, None] == jnp.arange(EXPERTS, dtype=jnp.int32)[None, None, :]).astype(jnp.int32)
    ranks = jnp.cumsum(member, axis=1) - member
    slot_of = lax.optimization_barrier(jnp.sum(ranks * member, axis=-1))
    block_ids = jnp.arange(blocks, dtype=jnp.int32)[:, None]
    per_expert = blocks * CAP
    position = (chosen * per_expert + block_ids * CAP + slot_of).reshape(-1).astype(jnp.int32)

    def to_experts(values):
        buffer = jnp.zeros((EXPERTS * per_expert, E), values.dtype).at[position].set(values)
        return buffer.reshape(EXPERTS, per_expert, E)

    def expert_forward(operands):
        rows, weight_in, weight_out = operands
        pre_act = jnp.dot(rows, weight_in, preferred_element_type=jnp.float32)
        hidden = jax.nn.silu(pre_act).astype(jnp.bfloat16)
        return column_partials(hidden, weight_out).astype(jnp.bfloat16)
    routed = to_experts(normed)
    expert_out = lax.map(expert_forward, (routed, w_in, w_out)).reshape(EXPERTS * per_expert, E)
    mixture = expert_out[position].astype(jnp.float32)
    joined = (normed.astype(jnp.float32) + mixture).astype(jnp.bfloat16)
    tower_pre = jnp.einsum('be,kem->kbm', joined.astype(jnp.float32), w_tow1.astype(jnp.float32))
    logits = lax.optimization_barrier(jnp.sum(jax.nn.silu(tower_pre) * w_tow2[:, None, :], axis=-1))
    predicted = jnp.stack([jax.nn.sigmoid(logits[0]), jax.nn.sigmoid(logits[1]), logits[2]], axis=-1)
    logit_grad = predicted - targets.reshape(-1, 3)
    tower_grad = (logit_grad.T[:, :, None] * w_tow2[:, None, :] * silu_slope(tower_pre)).astype(jnp.bfloat16)
    joined_grad = jnp.einsum('kbm,kem->be', tower_grad.astype(jnp.float32), w_tow1.astype(jnp.float32)).astype(jnp.bfloat16)

    def expert_backward(operands):
        rows, grads, weight_in, weight_out = operands
        pre_act = jnp.dot(rows, weight_in, preferred_element_type=jnp.float32)
        hidden = jax.nn.silu(pre_act).astype(jnp.bfloat16)
        grad_hidden = jnp.dot(grads, weight_out.T, preferred_element_type=jnp.float32)
        grad_pre = (grad_hidden * silu_slope(pre_act)).astype(jnp.bfloat16)
        grad_out = jnp.dot(hidden.T, grads, preferred_element_type=jnp.float32)
        grad_in = jnp.dot(rows.T, grad_pre, preferred_element_type=jnp.float32)
        input_grad = column_partials(grad_pre, weight_in.T).astype(jnp.bfloat16)
        return (grad_in, grad_out, input_grad)
    grad_w_in, grad_w_out, input_grad = lax.map(expert_backward, (routed, to_experts(joined_grad), w_in, w_out))
    mixture_grad = input_grad.reshape(EXPERTS * per_expert, E)[position].astype(jnp.float32)
    normed_grad = joined_grad.astype(jnp.float32) + mixture_grad
    scaled_grad = normed_grad * norm_gain
    summed_grad = inverse * (scaled_grad - summed * inverse * inverse * lax.optimization_barrier(jnp.mean(scaled_grad * summed, axis=-1, keepdims=True)))
    summed_grad = summed_grad.reshape(GROUPS, B_GROUP, E)

    def group_grad(group):
        group_values = summed_grad[group]

        def feature_grad(feature):
            pooled_grad = rounded(group_values * feat_gain[feature])
            terms = pooled_grad[:, None, :] * live_mask(bag_len[feature, group])[:, :, None]
            return jnp.zeros((WIN, E), jnp.float32).at[bag_idx[feature, group].reshape(-1)].add(terms.reshape(-1, E))
        return lax.map(feature_grad, feature_ids)
    window_grad = jnp.swapaxes(lax.map(group_grad, group_ids), 0, 1)

    def table_rows(operands):
        rows_grad, row_ids = operands
        return jnp.zeros((TROWS, E), jnp.float32).at[row_ids.reshape(-1)].add(rows_grad.reshape(-1, E))
    grad_table = lax.map(table_rows, (window_grad, windows))
    return (predicted.reshape(GROUPS, B_GROUP, 3), grad_table, grad_w_in, grad_w_out)
```

```python
import jax
import jax.numpy as jnp
from jax import lax
from jax.sharding import PartitionSpec as P

code_range = 127.0


def silu_slope(values):
    sigma = jax.nn.sigmoid(values)
    return sigma * (1.0 + values * (1.0 - sigma))


def bag_counts_t(indices, lengths, window):
    slots = jnp.arange(indices.shape[1], dtype=jnp.int32)
    live = jnp.where(slots[:, None] < lengths[None, :], indices.T, -1)
    positions = jnp.arange(window, dtype=jnp.int32)
    hits = (live[:, None, :] == positions[None, :, None]).astype(jnp.float32)
    return jnp.sum(hits, axis=0).astype(jnp.bfloat16)


def to_owners(rows, owners):
    shaped = rows.reshape(owners, rows.shape[0] // owners, rows.shape[-1])
    arrived = lax.all_to_all(shaped, "table", split_axis=0, concat_axis=0, tiled=True)
    return arrived.reshape(rows.shape)


def shard_partials(left, right, shards):
    rows, width = left.shape
    split_left = left.reshape(rows, shards, width // shards)
    split_right = right.reshape(shards, width // shards, right.shape[-1])
    partials = jnp.einsum("rkf,kfe->kre", split_left, split_right, preferred_element_type=jnp.float32)
    return jnp.sum(partials.astype(jnp.bfloat16).astype(jnp.float32), axis=0).astype(jnp.bfloat16)


def local(
    table,
    row_scale,
    windows,
    bag_idx,
    bag_len,
    feat_gain,
    norm_gain,
    expert_ids,
    w_in,
    w_out,
    w_tow1,
    w_tow2,
    targets,
):
    owners = lax.axis_size("table")
    samples = expert_ids.shape[1]
    capacity = max(2, 2 * samples // owners)
    local_rows = owners * capacity
    contract_rows = (((0,), (0,)), ((), ()))
    contract_cols = (((1,), (1,)), ((), ()))
    weight_in = w_in[0]
    weight_out = w_out[0]
    full_in = lax.all_gather(weight_in, "expert", axis=1, tiled=True)
    full_out = lax.all_gather(weight_out, "expert", axis=0, tiled=True)
    shards = full_in.shape[1] // weight_in.shape[1]

    window = windows[0, 0]
    picked = jnp.take(table[0], window, axis=0).astype(jnp.float32)
    scales = jnp.take(row_scale[0], window)
    dequant = (picked * scales[:, None] / code_range).astype(jnp.bfloat16)
    counts_t = bag_counts_t(bag_idx[0, 0], bag_len[0, 0], window.shape[0])
    pooled = lax.dot_general(
        counts_t, dequant, contract_rows, preferred_element_type=jnp.float32
    ).astype(jnp.bfloat16)
    features = lax.all_to_all(
        pooled.reshape(owners, samples, pooled.shape[-1]),
        "table",
        split_axis=0,
        concat_axis=0,
        tiled=True,
    )
    summed = jnp.sum(features.astype(jnp.float32) * feat_gain[:, None, :], axis=0)
    inverse = lax.rsqrt(jnp.mean(summed * summed, axis=-1, keepdims=True) + 1e-05)
    normed = (summed * inverse * norm_gain).astype(jnp.bfloat16)

    chosen = expert_ids[0, :, 0]
    member = (chosen[:, None] == jnp.arange(owners, dtype=jnp.int32)[None, :]).astype(jnp.int32)
    ranks = jnp.cumsum(member, axis=0) - member
    slot_of = jnp.sum(ranks * member, axis=1)
    target_slot = chosen * capacity + slot_of
    placing = (jnp.arange(local_rows, dtype=jnp.int32)[:, None] == target_slot[None, :]).astype(
        jnp.bfloat16
    )
    outgoing = jnp.dot(placing, normed, preferred_element_type=jnp.float32).astype(jnp.bfloat16)
    rows = to_owners(outgoing, owners)
    pre_act = jnp.dot(rows, full_in, preferred_element_type=jnp.float32)
    hidden = jax.nn.silu(pre_act).astype(jnp.bfloat16)
    expert_out = to_owners(shard_partials(hidden, full_out, shards), owners)
    mixture = lax.dot_general(
        placing, expert_out, contract_rows, preferred_element_type=jnp.float32
    )
    joined = (normed.astype(jnp.float32) + mixture).astype(jnp.bfloat16)
    tower_pre = jnp.einsum("be,kem->kbm", joined, w_tow1, preferred_element_type=jnp.float32)
    logits = jnp.sum(jax.nn.silu(tower_pre) * w_tow2[:, None, :], axis=-1)
    predicted = jnp.stack(
        [jax.nn.sigmoid(logits[0]), jax.nn.sigmoid(logits[1]), logits[2]], axis=-1
    )
    logit_grad = predicted - targets[0]
    tower_grad = (logit_grad.T[:, :, None] * w_tow2[:, None, :] * silu_slope(tower_pre)).astype(
        jnp.bfloat16
    )
    joined_grad = jnp.einsum(
        "kbm,kem->be", tower_grad, w_tow1, preferred_element_type=jnp.float32
    ).astype(jnp.bfloat16)
    back_rows = jnp.dot(placing, joined_grad, preferred_element_type=jnp.float32).astype(
        jnp.bfloat16
    )
    row_grads = to_owners(back_rows, owners)
    grad_hidden = lax.dot_general(
        row_grads, full_out, contract_cols, preferred_element_type=jnp.float32
    )
    grad_pre = (grad_hidden * silu_slope(pre_act)).astype(jnp.bfloat16)
    input_grad = to_owners(shard_partials(grad_pre, full_in.T, shards), owners)
    mixture_grad = lax.dot_general(
        placing, input_grad, contract_rows, preferred_element_type=jnp.float32
    )
    normed_grad = joined_grad.astype(jnp.float32) + mixture_grad
    scaled_grad = normed_grad * norm_gain
    summed_grad = inverse * (
        scaled_grad
        - summed * inverse * inverse * jnp.mean(scaled_grad * summed, axis=-1, keepdims=True)
    )
    feature_grad = (summed_grad[None, :, :] * feat_gain[:, None, :]).astype(jnp.bfloat16)
    returned = lax.all_to_all(
        feature_grad, "table", split_axis=0, concat_axis=0, tiled=True
    ).reshape(owners * samples, feature_grad.shape[-1])
    window_grad = jnp.dot(counts_t, returned, preferred_element_type=jnp.float32)
    row_select = (jnp.arange(table.shape[1], dtype=jnp.int32)[:, None] == window[None, :]).astype(
        jnp.float32
    )
    row_grad = jnp.dot(row_select, window_grad, precision=lax.Precision.HIGHEST)
    groups = lax.axis_size("expert")
    group_rows = lax.all_to_all(
        row_grad.reshape(groups, row_grad.shape[0] // groups, row_grad.shape[-1]),
        "expert",
        split_axis=0,
        concat_axis=0,
        tiled=True,
    )
    table_grad = jnp.sum(group_rows, axis=0)

    all_rows = lax.all_gather(rows, "expert", axis=0, tiled=True)
    all_grads = lax.all_gather(row_grads, "expert", axis=0, tiled=True)
    shard_pre = jnp.dot(all_rows, weight_in, preferred_element_type=jnp.float32)
    shard_hidden = jax.nn.silu(shard_pre).astype(jnp.bfloat16)
    shard_grad_hidden = lax.dot_general(
        all_grads, weight_out, contract_cols, preferred_element_type=jnp.float32
    )
    shard_grad_pre = (shard_grad_hidden * silu_slope(shard_pre)).astype(jnp.bfloat16)
    grad_out = lax.dot_general(
        shard_hidden, all_grads, contract_rows, preferred_element_type=jnp.float32
    )
    grad_in = lax.dot_general(
        all_rows, shard_grad_pre, contract_rows, preferred_element_type=jnp.float32
    )
    return (predicted[None], table_grad[None], grad_in[None], grad_out[None])


def solution(mesh):
    in_specs = (
        P("table", None, None),
        P("table", None),
        P("table", "expert", None),
        P("table", "expert", None, None),
        P("table", "expert", None),
        P(),
        P(),
        P("expert", "table", None),
        P("table", None, "expert"),
        P("table", "expert", None),
        P(),
        P(),
        P("expert", "table", None),
    )
    out_specs = (
        P("expert", "table", None),
        P("table", "expert", None),
        P("table", None, "expert"),
        P("table", "expert", None),
    )
    return jax.shard_map(local, mesh=mesh, in_specs=in_specs, out_specs=out_specs, check_vma=False)
```

```python
import jax
import jax.numpy as jnp
from jax import lax
from jax.sharding import PartitionSpec as P


code_range = 127.0


def silu_slope(values):
    sigma = jax.nn.sigmoid(values)
    return sigma * (1.0 + values * (1.0 - sigma))


def bag_counts_t(indices, lengths, window):
    slots = jnp.arange(indices.shape[1], dtype=jnp.int32)
    live = jnp.where(slots[:, None] < lengths[None, :], indices.T, -1)
    positions = jnp.arange(window, dtype=jnp.int32)
    hits = (live[:, None, :] == positions[None, :, None]).astype(jnp.float32)
    return jnp.sum(hits, axis=0).astype(jnp.bfloat16)


def to_owners(rows, owners):
    shaped = rows.reshape(owners, rows.shape[0] // owners, rows.shape[-1])
    arrived = lax.all_to_all(shaped, "table", split_axis=0, concat_axis=0, tiled=True)
    return arrived.reshape(rows.shape)


def shard_partials(left, right, shards):
    rows, width = left.shape
    split_left = left.reshape(rows, shards, width // shards)
    split_right = right.reshape(shards, width // shards, right.shape[-1])
    partials = jnp.einsum("rkf,kfe->kre", split_left, split_right, preferred_element_type=jnp.float32)
    return jnp.sum(partials.astype(jnp.bfloat16).astype(jnp.float32), axis=0).astype(jnp.bfloat16)


def step(
    table,
    row_scale,
    windows,
    bag_idx,
    bag_len,
    feat_gain,
    norm_gain,
    expert_ids,
    w_in,
    w_out,
    w_tow1,
    w_tow2,
    targets,
):
    owners = lax.axis_size("table")
    samples = expert_ids.shape[1]
    capacity = max(2, 2 * samples // owners)
    local_rows = owners * capacity
    contract_rows = (((0,), (0,)), ((), ()))
    contract_cols = (((1,), (1,)), ((), ()))
    weight_in = w_in[0]
    weight_out = w_out[0]
    full_in = lax.all_gather(weight_in, "expert", axis=1, tiled=True)
    full_out = lax.all_gather(weight_out, "expert", axis=0, tiled=True)
    shards = full_in.shape[1] // weight_in.shape[1]

    window = windows[0, 0]
    picked = jnp.take(table[0], window, axis=0).astype(jnp.float32)
    scales = jnp.take(row_scale[0], window)
    dequant = (picked * scales[:, None] / code_range).astype(jnp.bfloat16)
    counts_t = bag_counts_t(bag_idx[0, 0], bag_len[0, 0], window.shape[0])
    pooled = lax.dot_general(
        counts_t, dequant, contract_rows, preferred_element_type=jnp.float32
    ).astype(jnp.bfloat16)
    features = lax.all_to_all(
        pooled.reshape(owners, samples, pooled.shape[-1]),
        "table",
        split_axis=0,
        concat_axis=0,
        tiled=True,
    )
    summed = jnp.sum(features.astype(jnp.float32) * feat_gain[:, None, :], axis=0)
    inverse = lax.rsqrt(jnp.mean(summed * summed, axis=-1, keepdims=True) + 1e-05)
    normed = (summed * inverse * norm_gain).astype(jnp.bfloat16)

    chosen = expert_ids[0, :, 0]
    member = (chosen[:, None] == jnp.arange(owners, dtype=jnp.int32)[None, :]).astype(jnp.int32)
    ranks = jnp.cumsum(member, axis=0) - member
    slot_of = jnp.sum(ranks * member, axis=1)
    target_slot = chosen * capacity + slot_of
    placing = (jnp.arange(local_rows, dtype=jnp.int32)[:, None] == target_slot[None, :]).astype(
        jnp.bfloat16
    )
    outgoing = jnp.dot(placing, normed, preferred_element_type=jnp.float32).astype(jnp.bfloat16)
    rows = to_owners(outgoing, owners)
    all_rows = lax.all_gather(rows, "expert", axis=0, tiled=True)
    pre_act = jnp.dot(rows, full_in, preferred_element_type=jnp.float32)
    hidden = jax.nn.silu(pre_act).astype(jnp.bfloat16)
    expert_partial = shard_partials(hidden, full_out, shards)
    expert_out = to_owners(expert_partial, owners)
    mixture = lax.dot_general(
        placing, expert_out, contract_rows, preferred_element_type=jnp.float32
    )
    joined = (normed.astype(jnp.float32) + mixture).astype(jnp.bfloat16)
    tower_pre = jnp.einsum("be,kem->kbm", joined, w_tow1, preferred_element_type=jnp.float32)
    logits = jnp.sum(jax.nn.silu(tower_pre) * w_tow2[:, None, :], axis=-1)
    predicted = jnp.stack(
        [jax.nn.sigmoid(logits[0]), jax.nn.sigmoid(logits[1]), logits[2]], axis=-1
    )
    logit_grad = predicted - targets[0]
    tower_grad = (logit_grad.T[:, :, None] * w_tow2[:, None, :] * silu_slope(tower_pre)).astype(
        jnp.bfloat16
    )
    joined_grad = jnp.einsum(
        "kbm,kem->be", tower_grad, w_tow1, preferred_element_type=jnp.float32
    ).astype(jnp.bfloat16)
    back_rows = jnp.dot(placing, joined_grad, preferred_element_type=jnp.float32).astype(
        jnp.bfloat16
    )
    row_grads = to_owners(back_rows, owners)
    all_grads = lax.all_gather(row_grads, "expert", axis=0, tiled=True)
    grad_hidden = lax.dot_general(
        row_grads, full_out, contract_cols, preferred_element_type=jnp.float32
    )
    grad_pre = (grad_hidden * silu_slope(pre_act)).astype(jnp.bfloat16)
    input_partial = shard_partials(grad_pre, full_in.T, shards)
    input_grad = to_owners(input_partial, owners)
    mixture_grad = lax.dot_general(
        placing, input_grad, contract_rows, preferred_element_type=jnp.float32
    )
    normed_grad = joined_grad.astype(jnp.float32) + mixture_grad
    scaled_grad = normed_grad * norm_gain
    summed_grad = inverse * (
        scaled_grad
        - summed * inverse * inverse * jnp.mean(scaled_grad * summed, axis=-1, keepdims=True)
    )
    feature_grad = (summed_grad[None, :, :] * feat_gain[:, None, :]).astype(jnp.bfloat16)
    returned = lax.all_to_all(
        feature_grad, "table", split_axis=0, concat_axis=0, tiled=True
    ).reshape(owners * samples, feature_grad.shape[-1])
    window_grad = jnp.dot(counts_t, returned, preferred_element_type=jnp.float32)
    row_select = (jnp.arange(table.shape[1], dtype=jnp.int32)[:, None] == window[None, :]).astype(
        jnp.float32
    )
    row_grad = jnp.dot(row_select, window_grad, precision=lax.Precision.HIGHEST)
    groups = lax.axis_size("expert")
    group_rows = lax.all_to_all(
        row_grad.reshape(groups, row_grad.shape[0] // groups, row_grad.shape[-1]),
        "expert",
        split_axis=0,
        concat_axis=0,
        tiled=True,
    )
    table_grad = jnp.sum(group_rows, axis=0)

    shard_pre = jnp.dot(all_rows, weight_in, preferred_element_type=jnp.float32)
    shard_hidden = jax.nn.silu(shard_pre).astype(jnp.bfloat16)
    shard_grad_hidden = lax.dot_general(
        all_grads, weight_out, contract_cols, preferred_element_type=jnp.float32
    )
    shard_grad_pre = (shard_grad_hidden * silu_slope(shard_pre)).astype(jnp.bfloat16)
    grad_out = lax.dot_general(
        shard_hidden, all_grads, contract_rows, preferred_element_type=jnp.float32
    )
    grad_in = lax.dot_general(
        all_rows, shard_grad_pre, contract_rows, preferred_element_type=jnp.float32
    )
    return (predicted[None], table_grad[None], grad_in[None], grad_out[None])


def solution(mesh):
    in_specs = (
        P("table", None, None),
        P("table", None),
        P("table", "expert", None),
        P("table", "expert", None, None),
        P("table", "expert", None),
        P(),
        P(),
        P("expert", "table", None),
        P("table", None, "expert"),
        P("table", "expert", None),
        P(),
        P(),
        P("expert", "table", None),
    )
    out_specs = (
        P("expert", "table", None),
        P("table", "expert", None),
        P("table", None, "expert"),
        P("table", "expert", None),
    )
    return jax.shard_map(step, mesh=mesh, in_specs=in_specs, out_specs=out_specs, check_vma=False)
```

```python
import jax
import jax.numpy as jnp
from jax import lax
from jax.sharding import PartitionSpec as P


code_range = 127.0


def silu_slope(values):
    sigma = jax.nn.sigmoid(values)
    return sigma * (1.0 + values * (1.0 - sigma))


def bag_counts_t(indices, lengths, window):
    slots = jnp.arange(indices.shape[1], dtype=jnp.int32)
    live = jnp.where(slots[:, None] < lengths[None, :], indices.T, -1)
    positions = jnp.arange(window, dtype=jnp.int32)
    hits = (live[:, None, :] == positions[None, :, None]).astype(jnp.float32)
    return jnp.sum(hits, axis=0).astype(jnp.bfloat16)


def to_owners(rows, owners):
    shaped = rows.reshape(owners, rows.shape[0] // owners, rows.shape[-1])
    arrived = lax.all_to_all(shaped, "table", split_axis=0, concat_axis=0, tiled=True)
    return arrived.reshape(rows.shape)


def shard_partials(left, right, shards):
    rows, width = left.shape
    split_left = left.reshape(rows, shards, width // shards)
    split_right = right.reshape(shards, width // shards, right.shape[-1])
    partials = jnp.einsum("rkf,kfe->kre", split_left, split_right, preferred_element_type=jnp.float32)
    return jnp.sum(partials.astype(jnp.bfloat16).astype(jnp.float32), axis=0).astype(jnp.bfloat16)


def step(
    table,
    row_scale,
    windows,
    bag_idx,
    bag_len,
    feat_gain,
    norm_gain,
    expert_ids,
    w_in,
    w_out,
    w_tow1,
    w_tow2,
    targets,
):
    owners = lax.axis_size("table")
    samples = expert_ids.shape[1]
    capacity = max(2, 2 * samples // owners)
    local_rows = owners * capacity
    contract_rows = (((0,), (0,)), ((), ()))
    contract_cols = (((1,), (1,)), ((), ()))
    weight_in = w_in[0]
    weight_out = w_out[0]
    full_in = lax.all_gather(weight_in, "expert", axis=1, tiled=True)
    full_out = lax.all_gather(weight_out, "expert", axis=0, tiled=True)
    shards = full_in.shape[1] // weight_in.shape[1]

    window = windows[0, 0]
    picked = jnp.take(table[0], window, axis=0).astype(jnp.float32)
    scales = jnp.take(row_scale[0], window)
    dequant = (picked * scales[:, None] / code_range).astype(jnp.bfloat16)
    counts_t = bag_counts_t(bag_idx[0, 0], bag_len[0, 0], window.shape[0])
    pooled = lax.dot_general(
        counts_t, dequant, contract_rows, preferred_element_type=jnp.float32
    ).astype(jnp.bfloat16)
    features = lax.all_to_all(
        pooled.reshape(owners, samples, pooled.shape[-1]),
        "table",
        split_axis=0,
        concat_axis=0,
        tiled=True,
    )
    summed = jnp.sum(features.astype(jnp.float32) * feat_gain[:, None, :], axis=0)
    inverse = lax.rsqrt(jnp.mean(summed * summed, axis=-1, keepdims=True) + 1e-05)
    normed = (summed * inverse * norm_gain).astype(jnp.bfloat16)

    chosen = expert_ids[0, :, 0]
    member = (chosen[:, None] == jnp.arange(owners, dtype=jnp.int32)[None, :]).astype(jnp.int32)
    ranks = jnp.cumsum(member, axis=0) - member
    slot_of = jnp.sum(ranks * member, axis=1)
    target_slot = chosen * capacity + slot_of
    placing = (jnp.arange(local_rows, dtype=jnp.int32)[:, None] == target_slot[None, :]).astype(
        jnp.int32
    )
    source = jnp.sum(placing * jnp.arange(1, samples + 1, dtype=jnp.int32)[None, :], axis=1)
    width = normed.shape[-1]
    lanes = 128 * (-(-(width + 4) // 128))
    payload = jnp.concatenate(
        [
            normed.astype(jnp.float32),
            targets[0],
            jnp.ones((samples, 1), jnp.float32),
            jnp.zeros((samples, lanes - width - 4), jnp.float32),
        ],
        axis=1,
    )
    padded = jnp.concatenate([jnp.zeros((1, lanes), jnp.float32), payload], axis=0)
    arrived = to_owners(jnp.take(padded, source, axis=0), owners)
    rows = arrived[:, :width].astype(jnp.bfloat16)
    row_targets = arrived[:, width : width + 3]
    row_live = arrived[:, width + 3 : width + 4]
    all_rows = lax.all_gather(rows, "expert", axis=0, tiled=True)
    pre_act = jnp.dot(rows, full_in, preferred_element_type=jnp.float32)
    hidden = jax.nn.silu(pre_act).astype(jnp.bfloat16)
    mixture = shard_partials(hidden, full_out, shards)
    joined = (rows.astype(jnp.float32) + mixture.astype(jnp.float32)).astype(jnp.bfloat16)
    tower_pre = jnp.einsum("be,kem->kbm", joined, w_tow1, preferred_element_type=jnp.float32)
    logits = jnp.sum(jax.nn.silu(tower_pre) * w_tow2[:, None, :], axis=-1)
    predicted = jnp.stack(
        [jax.nn.sigmoid(logits[0]), jax.nn.sigmoid(logits[1]), logits[2]], axis=-1
    )
    logit_grad = (predicted - row_targets) * row_live
    tower_grad = (logit_grad.T[:, :, None] * w_tow2[:, None, :] * silu_slope(tower_pre)).astype(
        jnp.bfloat16
    )
    joined_grad = jnp.einsum(
        "kbm,kem->be", tower_grad, w_tow1, preferred_element_type=jnp.float32
    ).astype(jnp.bfloat16)
    row_grads = joined_grad
    all_grads = lax.all_gather(row_grads, "expert", axis=0, tiled=True)
    grad_hidden = lax.dot_general(
        row_grads, full_out, contract_cols, preferred_element_type=jnp.float32
    )
    grad_pre = (grad_hidden * silu_slope(pre_act)).astype(jnp.bfloat16)
    input_grad = shard_partials(grad_pre, full_in.T, shards)
    row_normed_grad = joined_grad.astype(jnp.float32) + input_grad.astype(jnp.float32)
    back = jnp.concatenate(
        [
            row_normed_grad,
            predicted,
            jnp.zeros((local_rows, lanes - width - 3), jnp.float32),
        ],
        axis=1,
    )
    mine = jnp.take(to_owners(back, owners), target_slot, axis=0)
    normed_grad = mine[:, :width]
    predicted = mine[:, width : width + 3]
    scaled_grad = normed_grad * norm_gain
    summed_grad = inverse * (
        scaled_grad
        - summed * inverse * inverse * jnp.mean(scaled_grad * summed, axis=-1, keepdims=True)
    )
    feature_grad = (summed_grad[None, :, :] * feat_gain[:, None, :]).astype(jnp.bfloat16)
    returned = lax.all_to_all(
        feature_grad, "table", split_axis=0, concat_axis=0, tiled=True
    ).reshape(owners * samples, feature_grad.shape[-1])
    window_grad = jnp.dot(counts_t, returned, preferred_element_type=jnp.float32)
    row_select = (jnp.arange(table.shape[1], dtype=jnp.int32)[:, None] == window[None, :]).astype(
        jnp.float32
    )
    row_grad = jnp.dot(row_select, window_grad, precision=lax.Precision.HIGHEST)
    groups = lax.axis_size("expert")
    group_rows = lax.all_to_all(
        row_grad.reshape(groups, row_grad.shape[0] // groups, row_grad.shape[-1]),
        "expert",
        split_axis=0,
        concat_axis=0,
        tiled=True,
    )
    table_grad = jnp.sum(group_rows, axis=0)

    shard_pre = jnp.dot(all_rows, weight_in, preferred_element_type=jnp.float32)
    shard_hidden = jax.nn.silu(shard_pre).astype(jnp.bfloat16)
    shard_grad_hidden = lax.dot_general(
        all_grads, weight_out, contract_cols, preferred_element_type=jnp.float32
    )
    shard_grad_pre = (shard_grad_hidden * silu_slope(shard_pre)).astype(jnp.bfloat16)
    grad_out = lax.dot_general(
        shard_hidden, all_grads, contract_rows, preferred_element_type=jnp.float32
    )
    grad_in = lax.dot_general(
        all_rows, shard_grad_pre, contract_rows, preferred_element_type=jnp.float32
    )
    return (predicted[None], table_grad[None], grad_in[None], grad_out[None])


def solution(mesh):
    in_specs = (
        P("table", None, None),
        P("table", None),
        P("table", "expert", None),
        P("table", "expert", None, None),
        P("table", "expert", None),
        P(),
        P(),
        P("expert", "table", None),
        P("table", None, "expert"),
        P("table", "expert", None),
        P(),
        P(),
        P("expert", "table", None),
    )
    out_specs = (
        P("expert", "table", None),
        P("table", "expert", None),
        P("table", None, "expert"),
        P("table", "expert", None),
    )
    return jax.shard_map(step, mesh=mesh, in_specs=in_specs, out_specs=out_specs, check_vma=False)
```

```python
import jax
import jax.numpy as jnp
from jax import lax
from jax.sharding import PartitionSpec as P


code_range = 127.0


def silu_slope(values):
    sigma = jax.nn.sigmoid(values)
    return sigma * (1.0 + values * (1.0 - sigma))


def bag_counts_t(indices, lengths, window):
    slots = jnp.arange(indices.shape[1], dtype=jnp.int32)
    live = jnp.where(slots[:, None] < lengths[None, :], indices.T, -1).astype(jnp.bfloat16)
    positions = jnp.arange(window, dtype=jnp.int32).astype(jnp.bfloat16)
    hits = (live[:, None, :] == positions[None, :, None]).astype(jnp.bfloat16)
    return jnp.sum(hits, axis=0, dtype=jnp.bfloat16)


def to_owners(rows, owners):
    shaped = rows.reshape(owners, rows.shape[0] // owners, rows.shape[-1])
    arrived = lax.all_to_all(shaped, "table", split_axis=0, concat_axis=0, tiled=True)
    return arrived.reshape(rows.shape)


def shard_partials(left, right, shards):
    rows, width = left.shape
    split_left = left.reshape(rows, shards, width // shards)
    split_right = right.reshape(shards, width // shards, right.shape[-1])
    partials = jnp.einsum("rkf,kfe->kre", split_left, split_right, preferred_element_type=jnp.float32)
    return jnp.sum(partials.astype(jnp.bfloat16).astype(jnp.float32), axis=0).astype(jnp.bfloat16)


def step(
    table,
    row_scale,
    windows,
    bag_idx,
    bag_len,
    feat_gain,
    norm_gain,
    expert_ids,
    w_in,
    w_out,
    w_tow1,
    w_tow2,
    targets,
):
    owners = lax.axis_size("table")
    samples = expert_ids.shape[1]
    capacity = max(2, 2 * samples // owners)
    local_rows = owners * capacity
    contract_rows = (((0,), (0,)), ((), ()))
    contract_cols = (((1,), (1,)), ((), ()))
    weight_in = w_in[0]
    weight_out = w_out[0]
    full_in = lax.all_gather(weight_in, "expert", axis=1, tiled=True)
    full_out = lax.all_gather(weight_out, "expert", axis=0, tiled=True)
    shards = full_in.shape[1] // weight_in.shape[1]

    window = windows[0, 0]
    picked = jnp.take(table[0], window, axis=0).astype(jnp.float32)
    scales = jnp.take(row_scale[0], window)
    dequant = (picked * scales[:, None] / code_range).astype(jnp.bfloat16)
    counts_t = bag_counts_t(bag_idx[0, 0], bag_len[0, 0], window.shape[0])
    pooled = lax.dot_general(
        counts_t, dequant, contract_rows, preferred_element_type=jnp.float32
    ).astype(jnp.bfloat16)
    features = lax.all_to_all(
        pooled.reshape(owners, samples, pooled.shape[-1]),
        "table",
        split_axis=0,
        concat_axis=0,
        tiled=True,
    )
    summed = jnp.sum(features.astype(jnp.float32) * feat_gain[:, None, :], axis=0)
    inverse = lax.rsqrt(jnp.mean(summed * summed, axis=-1, keepdims=True) + 1e-05)
    normed = (summed * inverse * norm_gain).astype(jnp.bfloat16)

    chosen = expert_ids[0, :, 0]
    member = (chosen[:, None] == jnp.arange(owners, dtype=jnp.int32)[None, :]).astype(jnp.int32)
    ranks = jnp.cumsum(member, axis=0) - member
    slot_of = jnp.sum(ranks * member, axis=1)
    target_slot = chosen * capacity + slot_of
    placing = (jnp.arange(local_rows, dtype=jnp.int32)[:, None] == target_slot[None, :]).astype(
        jnp.int32
    )
    source = jnp.sum(placing * jnp.arange(1, samples + 1, dtype=jnp.int32)[None, :], axis=1)
    width = normed.shape[-1]
    lanes = 128 * (-(-(width + 4) // 128))
    payload = jnp.concatenate(
        [
            normed.astype(jnp.float32),
            targets[0],
            jnp.ones((samples, 1), jnp.float32),
            jnp.zeros((samples, lanes - width - 4), jnp.float32),
        ],
        axis=1,
    )
    padded = jnp.concatenate([jnp.zeros((1, lanes), jnp.float32), payload], axis=0)
    arrived = to_owners(jnp.take(padded, source, axis=0), owners)
    rows = arrived[:, :width].astype(jnp.bfloat16)
    row_targets = arrived[:, width : width + 3]
    row_live = arrived[:, width + 3 : width + 4]
    all_rows = lax.all_gather(rows, "expert", axis=0, tiled=True)
    pre_act = jnp.dot(rows, full_in, preferred_element_type=jnp.float32)
    hidden = jax.nn.silu(pre_act).astype(jnp.bfloat16)
    mixture = shard_partials(hidden, full_out, shards)
    joined = (rows.astype(jnp.float32) + mixture.astype(jnp.float32)).astype(jnp.bfloat16)
    tower_pre = jnp.einsum("be,kem->kbm", joined, w_tow1, preferred_element_type=jnp.float32)
    logits = jnp.sum(jax.nn.silu(tower_pre) * w_tow2[:, None, :], axis=-1)
    predicted = jnp.stack(
        [jax.nn.sigmoid(logits[0]), jax.nn.sigmoid(logits[1]), logits[2]], axis=-1
    )
    logit_grad = (predicted - row_targets) * row_live
    tower_grad = (logit_grad.T[:, :, None] * w_tow2[:, None, :] * silu_slope(tower_pre)).astype(
        jnp.bfloat16
    )
    joined_grad = jnp.einsum(
        "kbm,kem->be", tower_grad, w_tow1, preferred_element_type=jnp.float32
    ).astype(jnp.bfloat16)
    row_grads = joined_grad
    all_grads = lax.all_gather(row_grads, "expert", axis=0, tiled=True)
    grad_hidden = lax.dot_general(
        row_grads, full_out, contract_cols, preferred_element_type=jnp.float32
    )
    grad_pre = (grad_hidden * silu_slope(pre_act)).astype(jnp.bfloat16)
    input_grad = shard_partials(grad_pre, full_in.T, shards)
    row_normed_grad = joined_grad.astype(jnp.float32) + input_grad.astype(jnp.float32)
    back = jnp.concatenate(
        [
            row_normed_grad,
            predicted,
            jnp.zeros((local_rows, lanes - width - 3), jnp.float32),
        ],
        axis=1,
    )
    mine = jnp.take(to_owners(back, owners), target_slot, axis=0)
    normed_grad = mine[:, :width]
    predicted = mine[:, width : width + 3]
    scaled_grad = normed_grad * norm_gain
    summed_grad = inverse * (
        scaled_grad
        - summed * inverse * inverse * jnp.mean(scaled_grad * summed, axis=-1, keepdims=True)
    )
    feature_grad = (summed_grad[None, :, :] * feat_gain[:, None, :]).astype(jnp.bfloat16)
    returned = lax.all_to_all(
        feature_grad, "table", split_axis=0, concat_axis=0, tiled=True
    ).reshape(owners * samples, feature_grad.shape[-1])
    window_grad = jnp.dot(counts_t, returned, preferred_element_type=jnp.float32)
    row_select = (jnp.arange(table.shape[1], dtype=jnp.int32)[:, None] == window[None, :]).astype(
        jnp.float32
    )
    row_grad = jnp.dot(row_select, window_grad, precision=lax.Precision.HIGHEST)
    groups = lax.axis_size("expert")
    group_rows = lax.all_to_all(
        row_grad.reshape(groups, row_grad.shape[0] // groups, row_grad.shape[-1]),
        "expert",
        split_axis=0,
        concat_axis=0,
        tiled=True,
    )
    table_grad = jnp.sum(group_rows, axis=0)

    shard_pre = jnp.dot(all_rows, weight_in, preferred_element_type=jnp.float32)
    shard_hidden = jax.nn.silu(shard_pre).astype(jnp.bfloat16)
    shard_grad_hidden = lax.dot_general(
        all_grads, weight_out, contract_cols, preferred_element_type=jnp.float32
    )
    shard_grad_pre = (shard_grad_hidden * silu_slope(shard_pre)).astype(jnp.bfloat16)
    grad_out = lax.dot_general(
        shard_hidden, all_grads, contract_rows, preferred_element_type=jnp.float32
    )
    grad_in = lax.dot_general(
        all_rows, shard_grad_pre, contract_rows, preferred_element_type=jnp.float32
    )
    return (predicted[None], table_grad[None], grad_in[None], grad_out[None])


def solution(mesh):
    in_specs = (
        P("table", None, None),
        P("table", None),
        P("table", "expert", None),
        P("table", "expert", None, None),
        P("table", "expert", None),
        P(),
        P(),
        P("expert", "table", None),
        P("table", None, "expert"),
        P("table", "expert", None),
        P(),
        P(),
        P("expert", "table", None),
    )
    out_specs = (
        P("expert", "table", None),
        P("table", "expert", None),
        P("table", None, "expert"),
        P("table", "expert", None),
    )
    return jax.shard_map(step, mesh=mesh, in_specs=in_specs, out_specs=out_specs, check_vma=False)
```

```python
import jax
import jax.numpy as jnp
from jax import lax
from jax.sharding import PartitionSpec as P

code_range = 127.0


def silu_slope(values):
    sigma = jax.nn.sigmoid(values)
    return sigma * (1.0 + values * (1.0 - sigma))


def bag_counts_t(indices, lengths, window):
    slots = jnp.arange(indices.shape[1], dtype=jnp.int32)
    live = jnp.where(slots[:, None] < lengths[None, :], indices.T, -1)
    positions = jnp.arange(window, dtype=jnp.int32)
    hits = (live[:, None, :] == positions[None, :, None]).astype(jnp.float32)
    return jnp.sum(hits, axis=0).astype(jnp.bfloat16)


def to_owners(rows, owners):
    shaped = rows.reshape(owners, rows.shape[0] // owners, rows.shape[-1])
    arrived = lax.all_to_all(shaped, "table", split_axis=0, concat_axis=0, tiled=True)
    return arrived.reshape(rows.shape)


def ring_gather(value, axis_name):
    size = lax.axis_size(axis_name)
    parts = [value]
    for shift in range(1, size):
        pairs = [(i, (i + shift) % size) for i in range(size)]
        parts.append(lax.ppermute(value, axis_name, pairs))
    return jnp.stack(parts)


def sum_partials(partials):
    return jnp.sum(partials.astype(jnp.bfloat16).astype(jnp.float32), axis=0).astype(jnp.bfloat16)


def step(
    table,
    row_scale,
    windows,
    bag_idx,
    bag_len,
    feat_gain,
    norm_gain,
    expert_ids,
    w_in,
    w_out,
    w_tow1,
    w_tow2,
    targets,
):
    owners = lax.axis_size("table")
    samples = expert_ids.shape[1]
    capacity = max(2, 2 * samples // owners)
    local_rows = owners * capacity
    contract_rows = (((0,), (0,)), ((), ()))
    contract_cols = (((1,), (1,)), ((), ()))
    weight_in = w_in[0]
    weight_out = w_out[0]
    stacked_in = ring_gather(weight_in, "expert")
    stacked_out = ring_gather(weight_out, "expert")

    window = windows[0, 0]
    picked = jnp.take(table[0], window, axis=0).astype(jnp.float32)
    scales = jnp.take(row_scale[0], window)
    dequant = (picked * scales[:, None] / code_range).astype(jnp.bfloat16)
    counts_t = bag_counts_t(bag_idx[0, 0], bag_len[0, 0], window.shape[0])
    pooled = lax.dot_general(
        counts_t, dequant, contract_rows, preferred_element_type=jnp.float32
    ).astype(jnp.bfloat16)
    features = lax.all_to_all(
        pooled.reshape(owners, samples, pooled.shape[-1]),
        "table",
        split_axis=0,
        concat_axis=0,
        tiled=True,
    )
    summed = jnp.sum(features.astype(jnp.float32) * feat_gain[:, None, :], axis=0)
    inverse = lax.rsqrt(jnp.mean(summed * summed, axis=-1, keepdims=True) + 1e-05)
    normed = (summed * inverse * norm_gain).astype(jnp.bfloat16)

    chosen = expert_ids[0, :, 0]
    member = (chosen[:, None] == jnp.arange(owners, dtype=jnp.int32)[None, :]).astype(jnp.int32)
    ranks = jnp.cumsum(member, axis=0) - member
    slot_of = jnp.sum(ranks * member, axis=1)
    target_slot = chosen * capacity + slot_of
    placing = (jnp.arange(local_rows, dtype=jnp.int32)[:, None] == target_slot[None, :]).astype(
        jnp.int32
    )
    source = jnp.sum(placing * jnp.arange(1, samples + 1, dtype=jnp.int32)[None, :], axis=1)
    width = normed.shape[-1]
    lanes = 128 * (-(-(width + 4) // 128))
    payload = jnp.concatenate(
        [
            normed.astype(jnp.float32),
            targets[0],
            jnp.ones((samples, 1), jnp.float32),
            jnp.zeros((samples, lanes - width - 4), jnp.float32),
        ],
        axis=1,
    )
    padded = jnp.concatenate([jnp.zeros((1, lanes), jnp.float32), payload], axis=0)
    arrived = to_owners(jnp.take(padded, source, axis=0), owners)
    rows = arrived[:, :width].astype(jnp.bfloat16)
    row_targets = arrived[:, width : width + 3]
    row_live = arrived[:, width + 3 : width + 4]
    all_rows = ring_gather(rows, "expert").reshape(-1, rows.shape[-1])
    pre_act = jnp.einsum("re,kef->rkf", rows, stacked_in, preferred_element_type=jnp.float32)
    hidden = jax.nn.silu(pre_act).astype(jnp.bfloat16)
    mixture = sum_partials(
        jnp.einsum("rkf,kfe->kre", hidden, stacked_out, preferred_element_type=jnp.float32)
    )
    joined = (rows.astype(jnp.float32) + mixture.astype(jnp.float32)).astype(jnp.bfloat16)
    tower_pre = jnp.einsum("be,kem->kbm", joined, w_tow1, preferred_element_type=jnp.float32)
    logits = jnp.sum(jax.nn.silu(tower_pre) * w_tow2[:, None, :], axis=-1)
    predicted = jnp.stack(
        [jax.nn.sigmoid(logits[0]), jax.nn.sigmoid(logits[1]), logits[2]], axis=-1
    )
    logit_grad = (predicted - row_targets) * row_live
    tower_grad = (logit_grad.T[:, :, None] * w_tow2[:, None, :] * silu_slope(tower_pre)).astype(
        jnp.bfloat16
    )
    joined_grad = jnp.einsum(
        "kbm,kem->be", tower_grad, w_tow1, preferred_element_type=jnp.float32
    ).astype(jnp.bfloat16)
    row_grads = joined_grad
    all_grads = ring_gather(row_grads, "expert").reshape(-1, row_grads.shape[-1])
    grad_hidden = jnp.einsum(
        "re,kfe->rkf", row_grads, stacked_out, preferred_element_type=jnp.float32
    )
    grad_pre = (grad_hidden * silu_slope(pre_act)).astype(jnp.bfloat16)
    input_grad = sum_partials(
        jnp.einsum("rkf,kef->kre", grad_pre, stacked_in, preferred_element_type=jnp.float32)
    )
    row_normed_grad = joined_grad.astype(jnp.float32) + input_grad.astype(jnp.float32)
    back = jnp.concatenate(
        [
            row_normed_grad,
            predicted,
            jnp.zeros((local_rows, lanes - width - 3), jnp.float32),
        ],
        axis=1,
    )
    mine = jnp.take(to_owners(back, owners), target_slot, axis=0)
    normed_grad = mine[:, :width]
    predicted = mine[:, width : width + 3]
    scaled_grad = normed_grad * norm_gain
    summed_grad = inverse * (
        scaled_grad
        - summed * inverse * inverse * jnp.mean(scaled_grad * summed, axis=-1, keepdims=True)
    )
    feature_grad = (summed_grad[None, :, :] * feat_gain[:, None, :]).astype(jnp.bfloat16)
    returned = lax.all_to_all(
        feature_grad, "table", split_axis=0, concat_axis=0, tiled=True
    ).reshape(owners * samples, feature_grad.shape[-1])
    window_grad = jnp.dot(counts_t, returned, preferred_element_type=jnp.float32)
    row_select = (jnp.arange(table.shape[1], dtype=jnp.int32)[:, None] == window[None, :]).astype(
        jnp.float32
    )
    row_grad = jnp.dot(row_select, window_grad, precision=lax.Precision.HIGHEST)
    groups = lax.axis_size("expert")
    group_rows = lax.all_to_all(
        row_grad.reshape(groups, row_grad.shape[0] // groups, row_grad.shape[-1]),
        "expert",
        split_axis=0,
        concat_axis=0,
        tiled=True,
    )
    table_grad = jnp.sum(group_rows, axis=0)

    shard_pre = jnp.dot(all_rows, weight_in, preferred_element_type=jnp.float32)
    shard_hidden = jax.nn.silu(shard_pre).astype(jnp.bfloat16)
    shard_grad_hidden = lax.dot_general(
        all_grads, weight_out, contract_cols, preferred_element_type=jnp.float32
    )
    shard_grad_pre = (shard_grad_hidden * silu_slope(shard_pre)).astype(jnp.bfloat16)
    grad_out = lax.dot_general(
        shard_hidden, all_grads, contract_rows, preferred_element_type=jnp.float32
    )
    grad_in = lax.dot_general(
        all_rows, shard_grad_pre, contract_rows, preferred_element_type=jnp.float32
    )
    return (predicted[None], table_grad[None], grad_in[None], grad_out[None])


def solution(mesh):
    in_specs = (
        P("table", None, None),
        P("table", None),
        P("table", "expert", None),
        P("table", "expert", None, None),
        P("table", "expert", None),
        P(),
        P(),
        P("expert", "table", None),
        P("table", None, "expert"),
        P("table", "expert", None),
        P(),
        P(),
        P("expert", "table", None),
    )
    out_specs = (
        P("expert", "table", None),
        P("table", "expert", None),
        P("table", None, "expert"),
        P("table", "expert", None),
    )
    return jax.shard_map(step, mesh=mesh, in_specs=in_specs, out_specs=out_specs, check_vma=False)
```

```python
import jax
import jax.numpy as jnp
from jax import lax
from jax.sharding import PartitionSpec as P

code_range = 127.0


def silu_slope(values):
    sigma = jax.nn.sigmoid(values)
    return sigma * (1.0 + values * (1.0 - sigma))


def bag_counts_t(indices, lengths, window):
    slots = jnp.arange(indices.shape[1], dtype=jnp.int32)
    live = jnp.where(slots[:, None] < lengths[None, :], indices.T, -1)
    positions = jnp.arange(window, dtype=jnp.int32)
    hits = (live[:, None, :] == positions[None, :, None]).astype(jnp.float32)
    return jnp.sum(hits, axis=0).astype(jnp.bfloat16)


def to_owners(rows, owners):
    shaped = rows.reshape(owners, rows.shape[0] // owners, rows.shape[-1])
    arrived = lax.all_to_all(shaped, "table", split_axis=0, concat_axis=0, tiled=True)
    return arrived.reshape(rows.shape)


def ring_gather(value, axis_name):
    size = lax.axis_size(axis_name)
    parts = [value]
    for shift in range(1, size):
        pairs = [(i, (i + shift) % size) for i in range(size)]
        parts.append(lax.ppermute(value, axis_name, pairs))
    return jnp.stack(parts)


def sum_partials(partials):
    return jnp.sum(partials.astype(jnp.bfloat16).astype(jnp.float32), axis=0).astype(jnp.bfloat16)


def step(
    table,
    row_scale,
    windows,
    bag_idx,
    bag_len,
    feat_gain,
    norm_gain,
    expert_ids,
    w_in,
    w_out,
    w_tow1,
    w_tow2,
    targets,
):
    owners = lax.axis_size("table")
    samples = expert_ids.shape[1]
    capacity = max(2, 2 * samples // owners)
    local_rows = owners * capacity
    contract_rows = (((0,), (0,)), ((), ()))
    contract_cols = (((1,), (1,)), ((), ()))
    weight_in = w_in[0]
    weight_out = w_out[0]
    stacked_in = ring_gather(weight_in, "expert")
    stacked_out = ring_gather(weight_out, "expert")

    window = windows[0, 0]
    picked = jnp.take(table[0], window, axis=0).astype(jnp.float32)
    scales = jnp.take(row_scale[0], window)
    dequant = (picked * scales[:, None] / code_range).astype(jnp.bfloat16)
    counts_t = bag_counts_t(bag_idx[0, 0], bag_len[0, 0], window.shape[0])
    pooled = lax.dot_general(
        counts_t, dequant, contract_rows, preferred_element_type=jnp.float32
    ).astype(jnp.bfloat16)
    features = lax.all_to_all(
        pooled.reshape(owners, samples, pooled.shape[-1]),
        "table",
        split_axis=0,
        concat_axis=0,
        tiled=True,
    )
    summed = jnp.sum(features.astype(jnp.float32) * feat_gain[:, None, :], axis=0)
    inverse = lax.rsqrt(jnp.mean(summed * summed, axis=-1, keepdims=True) + 1e-05)
    normed = (summed * inverse * norm_gain).astype(jnp.bfloat16)

    chosen = expert_ids[0, :, 0]
    member = (chosen[:, None] == jnp.arange(owners, dtype=jnp.int32)[None, :]).astype(jnp.int32)
    ranks = jnp.cumsum(member, axis=0) - member
    slot_of = jnp.sum(ranks * member, axis=1)
    target_slot = chosen * capacity + slot_of
    placing = (jnp.arange(local_rows, dtype=jnp.int32)[:, None] == target_slot[None, :]).astype(
        jnp.int32
    )
    source = jnp.sum(placing * jnp.arange(1, samples + 1, dtype=jnp.int32)[None, :], axis=1)
    width = normed.shape[-1]
    lanes = 128 * (-(-(width + 4) // 128))
    extra = 128
    labels = jnp.concatenate(
        [
            targets[0],
            jnp.ones((samples, 1), jnp.float32),
            jnp.zeros((samples, extra - 4), jnp.float32),
        ],
        axis=1,
    )
    padded_labels = jnp.concatenate([jnp.zeros((1, extra), jnp.float32), labels], axis=0)
    row_labels = to_owners(jnp.take(padded_labels, source, axis=0), owners)
    row_targets = row_labels[:, :3]
    row_live = row_labels[:, 3:4]
    padded = jnp.concatenate([jnp.zeros((1, width), normed.dtype), normed], axis=0)
    rows = to_owners(jnp.take(padded, source, axis=0), owners)
    all_rows = ring_gather(rows, "expert").reshape(-1, rows.shape[-1])
    pre_act = jnp.einsum("re,kef->rkf", rows, stacked_in, preferred_element_type=jnp.float32)
    hidden = jax.nn.silu(pre_act).astype(jnp.bfloat16)
    mixture = sum_partials(
        jnp.einsum("rkf,kfe->kre", hidden, stacked_out, preferred_element_type=jnp.float32)
    )
    joined = (rows.astype(jnp.float32) + mixture.astype(jnp.float32)).astype(jnp.bfloat16)
    tower_pre = jnp.einsum("be,kem->kbm", joined, w_tow1, preferred_element_type=jnp.float32)
    logits = jnp.sum(jax.nn.silu(tower_pre) * w_tow2[:, None, :], axis=-1)
    predicted = jnp.stack(
        [jax.nn.sigmoid(logits[0]), jax.nn.sigmoid(logits[1]), logits[2]], axis=-1
    )
    logit_grad = (predicted - row_targets) * row_live
    tower_grad = (logit_grad.T[:, :, None] * w_tow2[:, None, :] * silu_slope(tower_pre)).astype(
        jnp.bfloat16
    )
    joined_grad = jnp.einsum(
        "kbm,kem->be", tower_grad, w_tow1, preferred_element_type=jnp.float32
    ).astype(jnp.bfloat16)
    row_grads = joined_grad
    all_grads = ring_gather(row_grads, "expert").reshape(-1, row_grads.shape[-1])
    grad_hidden = jnp.einsum(
        "re,kfe->rkf", row_grads, stacked_out, preferred_element_type=jnp.float32
    )
    grad_pre = (grad_hidden * silu_slope(pre_act)).astype(jnp.bfloat16)
    input_grad = sum_partials(
        jnp.einsum("rkf,kef->kre", grad_pre, stacked_in, preferred_element_type=jnp.float32)
    )
    row_normed_grad = joined_grad.astype(jnp.float32) + input_grad.astype(jnp.float32)
    back = jnp.concatenate(
        [
            row_normed_grad,
            predicted,
            jnp.zeros((local_rows, lanes - width - 3), jnp.float32),
        ],
        axis=1,
    )
    mine = jnp.take(to_owners(back, owners), target_slot, axis=0)
    normed_grad = mine[:, :width]
    predicted = mine[:, width : width + 3]
    scaled_grad = normed_grad * norm_gain
    summed_grad = inverse * (
        scaled_grad
        - summed * inverse * inverse * jnp.mean(scaled_grad * summed, axis=-1, keepdims=True)
    )
    feature_grad = (summed_grad[None, :, :] * feat_gain[:, None, :]).astype(jnp.bfloat16)
    returned = lax.all_to_all(
        feature_grad, "table", split_axis=0, concat_axis=0, tiled=True
    ).reshape(owners * samples, feature_grad.shape[-1])
    window_grad = jnp.dot(counts_t, returned, preferred_element_type=jnp.float32)
    row_select = (jnp.arange(table.shape[1], dtype=jnp.int32)[:, None] == window[None, :]).astype(
        jnp.float32
    )
    row_grad = jnp.dot(row_select, window_grad, precision=lax.Precision.HIGHEST)
    groups = lax.axis_size("expert")
    group_rows = lax.all_to_all(
        row_grad.reshape(groups, row_grad.shape[0] // groups, row_grad.shape[-1]),
        "expert",
        split_axis=0,
        concat_axis=0,
        tiled=True,
    )
    table_grad = jnp.sum(group_rows, axis=0)

    shard_pre = jnp.dot(all_rows, weight_in, preferred_element_type=jnp.float32)
    shard_hidden = jax.nn.silu(shard_pre).astype(jnp.bfloat16)
    shard_grad_hidden = lax.dot_general(
        all_grads, weight_out, contract_cols, preferred_element_type=jnp.float32
    )
    shard_grad_pre = (shard_grad_hidden * silu_slope(shard_pre)).astype(jnp.bfloat16)
    grad_out = lax.dot_general(
        shard_hidden, all_grads, contract_rows, preferred_element_type=jnp.float32
    )
    grad_in = lax.dot_general(
        all_rows, shard_grad_pre, contract_rows, preferred_element_type=jnp.float32
    )
    return (predicted[None], table_grad[None], grad_in[None], grad_out[None])


def solution(mesh):
    in_specs = (
        P("table", None, None),
        P("table", None),
        P("table", "expert", None),
        P("table", "expert", None, None),
        P("table", "expert", None),
        P(),
        P(),
        P("expert", "table", None),
        P("table", None, "expert"),
        P("table", "expert", None),
        P(),
        P(),
        P("expert", "table", None),
    )
    out_specs = (
        P("expert", "table", None),
        P("table", "expert", None),
        P("table", None, "expert"),
        P("table", "expert", None),
    )
    return jax.shard_map(step, mesh=mesh, in_specs=in_specs, out_specs=out_specs, check_vma=False)
```
